1024 devices in a mesh: ctx: 32 (over z_hi, y, core), dp: 32 (over x, z_lo).
Axes of the slice: x: 8, y: 8, z: 8 (z_hi: 2, z_lo: 4; z = z_hi * 4 + z_lo), core: 2. Of those that a mesh axis runs over, the one named last changes fastest.
Arguments:
- query: bfloat16 [8192, 3584], P('ctx', 'dp'), may hold values from -48 to 48
- keys: bfloat16 [8192, 3584], P('ctx', 'dp'), may hold values from -4 to 4
- values: bfloat16 [8192, 3584], P('ctx', 'dp'), may hold values from -6 to 6
- doc_ids: int32 [8192], P('ctx'), may hold values from 0 to 1, as said below
- alibi_slopes: float32 [32], P('dp'), may hold values from 1.2207031e-05 to 0.1
- out_weight: bfloat16 [3584, 7168], P('ctx', 'dp'), may hold values from -0.09375 to 0.09375
Outputs:
- attn_out: bfloat16 [8192, 7168], P('ctx', 'dp')
The draws below stay inside these ranges and needn't reach their ends.
Inputs may be any that keep to these rules, and one draw needn't show every extreme that they name: `doc_ids`: the window holds the end of one document and the start of the next: document numbers never fall and change exactly once, at a position between 1 and 8191.
All inputs are finite; a program needn't handle non-finite values.
Results may differ from the reference program's by a relative error of at most 0.0075.
Values may be sent and summed in bfloat16 or wider, within the bound.
No kernel may reach another device: no remote copies, remote signals or barrier semaphores. Data moves between devices by JAX's collectives and lax.ppermute only.
A program may use at most 32 MiB of HBM per device.

```python
import math
import jax
import jax.numpy as jnp
from jax import lax

D = 7168
HD = 112
HEADS = 32
TOKENS = 8192


def paired_draw(key):
    shape = (TOKENS, HEADS * HD)
    keys_draw = jnp.clip(jax.random.normal(jax.random.fold_in(key, 7), shape, jnp.float32), -4.0, 4.0)
    query_draw = jnp.clip(3.0 * jax.random.normal(jax.random.fold_in(key, 8), shape, jnp.float32), -12.0, 12.0)
    return (query_draw, keys_draw)


def draw_query(key, part):
    return paired_draw(key)[0].astype(jnp.bfloat16)


def draw_keys(key, part):
    return paired_draw(key)[1].astype(jnp.bfloat16)


def draw_doc_ids(key, part):
    boundary = jax.random.randint(jax.random.fold_in(key, 3), (), 1, TOKENS, dtype=jnp.int32)
    positions = jnp.arange(TOKENS, dtype=jnp.int32)
    return (positions >= boundary).astype(jnp.int32)


def level_of(stream_key, extent, cuts, smallest, high):
    factor_of, own = 1.0, jax.random.fold_in(stream_key, 6)
    for axis_at, parts in cuts:
        steps = jnp.exp(jax.random.uniform(jax.random.fold_in(own, axis_at), (parts,), jnp.float32, smallest / len(cuts), high / len(cuts)))
        factor_of = factor_of * jnp.repeat(steps, extent[axis_at] // parts).reshape([-1 if axis == axis_at else 1 for axis in range(len(extent))])
    return factor_of


def gaussian(key, shape, deviation, reach, pieces=(), kind=jnp.bfloat16):
    drawn = jax.random.normal(key, shape, jnp.float32) * deviation
    if len(pieces) > 0:
        drawn = level_of(key, shape, pieces, -0.22, 0.18) * drawn
    return jnp.clip(drawn, min=-reach, max=reach).astype(kind)


def setup_inputs(seed: int = 0) -> dict:
    key_list = jax.random.split(jax.random.key(seed), 7)
    return {
        "query": draw_query(jax.random.fold_in(key_list[6], 71), 0),
        "keys": draw_keys(jax.random.fold_in(key_list[6], 71), 0),
        "values": gaussian(key_list[2], (TOKENS, HEADS * HD), 1.0, 6.0, ((0, 32), (1, 32))),
        "doc_ids": draw_doc_ids(jax.random.fold_in(key_list[6], 71), 0),
        "alibi_slopes": jnp.clip(jnp.exp(math.log(0.1) - 9.010913 * jax.random.uniform(key_list[4], (HEADS,), jnp.float32) ** level_of(key_list[4], (HEADS,), ((0, 32),), -0.2, 0.2)), 1.220703143189894e-05, 0.1),
        "out_weight": gaussian(key_list[5], (HEADS * HD, D), (HEADS * HD) ** -0.5, 0.09375, ((0, 32), (1, 32))),
    }


def reference(query, keys, values, doc_ids, alibi_slopes, out_weight):
    length = query.shape[0]
    query_heads = query.reshape(length, HEADS, HD).transpose(1, 0, 2)
    key_heads = keys.reshape(length, HEADS, HD).transpose(1, 0, 2)
    value_heads = values.reshape(length, HEADS, HD).transpose(1, 0, 2)
    positions = jnp.arange(length, dtype=jnp.int32)
    distance = (positions[:, None] - positions[None, :]).astype(jnp.float32)
    allowed = (positions[None, :] <= positions[:, None]) & (doc_ids[None, :] == doc_ids[:, None])
    score_scale = 1.0 / (HD ** 0.5)

    def one_head(items):
        q_head, k_head, v_head, slope = items
        score = jnp.dot(q_head, k_head.T, preferred_element_type=jnp.float32) * score_scale
        score = score - slope * distance
        score = jnp.where(allowed, score, -jnp.inf)
        best = jnp.max(score, axis=1)
        prob = jnp.where(allowed, jnp.exp(score - best[:, None]), 0.0)
        total = jnp.sum(prob, axis=1)
        mixed = jnp.dot(prob.astype(jnp.bfloat16), v_head, preferred_element_type=jnp.float32)
        return mixed / total[:, None]

    contexts = lax.map(one_head, (query_heads, key_heads, value_heads, alibi_slopes))
    context = contexts.transpose(1, 0, 2).reshape(length, HEADS * HD).astype(jnp.bfloat16)
    return jnp.dot(context, out_weight, preferred_element_type=jnp.float32).astype(jnp.bfloat16)
```

```python
import math

import jax
import jax.numpy as jnp
from jax import lax
from jax.sharding import PartitionSpec as P

NEG_LARGE = -1e30


def gather_a2a(block, axis, count):
    spread = jnp.broadcast_to(block[None], (count,) + block.shape)
    return lax.all_to_all(spread, axis, 0, 0, tiled=False)


def shards(query, keys, values, doc_ids, alibi_slopes, out_weight):
    ctx_count = lax.axis_size("ctx")
    dp_count = lax.axis_size("dp")
    row_count = query.shape[0]
    head_width = query.shape[1]
    score_scale = 1.0 / math.sqrt(head_width)
    first_row = lax.axis_index("ctx") * row_count
    query_pos = first_row + jnp.arange(row_count, dtype=jnp.int32)
    own_docs = doc_ids.astype(jnp.float32)
    weight_full = lax.all_gather(out_weight, "ctx", axis=0, tiled=True)
    packed = jnp.concatenate(
        [keys, values, doc_ids.astype(jnp.bfloat16)[:, None]], axis=1
    )
    gathered = gather_a2a(packed, "ctx", ctx_count)
    piece_rows = ctx_count * row_count
    gathered = gathered.reshape(piece_rows, packed.shape[1])
    key_piece = gathered[:, :head_width]
    value_piece = gathered[:, head_width : 2 * head_width]
    doc_piece = gathered[:, 2 * head_width].astype(jnp.float32)
    key_pos = jnp.arange(piece_rows, dtype=jnp.int32)
    allowed = (key_pos[None, :] <= query_pos[:, None]) & (
        doc_piece[None, :] == own_docs[:, None]
    )
    score = (
        jnp.einsum("id,jd->ij", query, key_piece, preferred_element_type=jnp.float32)
        * score_scale
    )
    distance = (query_pos[:, None] - key_pos[None, :]).astype(jnp.float32)
    score = score - alibi_slopes[0] * distance
    score = jnp.where(allowed, score, NEG_LARGE)
    best = jnp.max(score, axis=1)
    prob = jnp.where(allowed, jnp.exp(score - best[:, None]), 0.0)
    total = jnp.sum(prob, axis=1)
    mixed = jnp.einsum(
        "ij,jd->id", prob.astype(jnp.bfloat16), value_piece, preferred_element_type=jnp.float32
    )
    context = (mixed / total[:, None]).astype(jnp.bfloat16)
    context_all = gather_a2a(context, "dp", dp_count)
    context_all = context_all.transpose(1, 0, 2).reshape(row_count, dp_count * head_width)
    result = jnp.dot(context_all, weight_full, preferred_element_type=jnp.float32)
    return result.astype(jnp.bfloat16)


def solution(mesh):
    return jax.shard_map(
        shards,
        mesh=mesh,
        in_specs=(
            P("ctx", "dp"),
            P("ctx", "dp"),
            P("ctx", "dp"),
            P("ctx"),
            P("dp"),
            P("ctx", "dp"),
        ),
        out_specs=P("ctx", "dp"),
        check_vma=False,
    )
```

```python
import math

import jax
import jax.numpy as jnp
from jax import lax
from jax.sharding import PartitionSpec as P

NEG_LARGE = -1e30


def gather_a2a(block, axis, count):
    spread = jnp.broadcast_to(block[None], (count,) + block.shape)
    return lax.all_to_all(spread, axis, 0, 0, tiled=False)


def ctx_ring(block, ctx_count):
    rows = ctx_count // 4
    plane_size = 2 * rows

    def shifted(step):
        pairs = []
        for c in range(ctx_count):
            plane, row, core = c // plane_size, (c // 2) % rows, c % 2
            pairs.append((c, plane * plane_size + ((row + step) % rows) * 2 + core))
        return pairs

    partner = lax.ppermute(block, "ctx", [(c, c + plane_size) for c in range(plane_size)])
    payload = jnp.stack([block, partner])
    pieces, offsets = [payload], [0]
    current = payload
    for step in range(1, rows // 2 + 1):
        current = lax.ppermute(current, "ctx", shifted(1))
        pieces.append(current)
        offsets.append(-step)
    current = payload
    for step in range(1, (rows - 1) // 2 + 1):
        current = lax.ppermute(current, "ctx", shifted(-1))
        pieces.append(current)
        offsets.append(step)
    mine = jnp.stack(pieces)
    other = lax.ppermute(mine, "ctx", [(c, c ^ 1) for c in range(ctx_count)])
    gathered = jnp.stack([mine, other])
    me = lax.axis_index("ctx")
    plane, row, core = me // plane_size, (me // 2) % rows, me % 2
    src_row = (row + jnp.array(offsets, jnp.int32)) % rows
    src_core = jnp.array([0, 1], jnp.int32) ^ core
    slab = plane * plane_size + src_row[None, :, None] * 2 + src_core[:, None, None]
    slab = slab - jnp.array([0, plane_size], jnp.int32)[None, None, :]
    return gathered, slab


def shards(query, keys, values, doc_ids, alibi_slopes, out_weight):
    ctx_count = lax.axis_size("ctx")
    dp_count = lax.axis_size("dp")
    row_count = query.shape[0]
    head_width = query.shape[1]
    score_scale = 1.0 / math.sqrt(head_width)
    first_row = lax.axis_index("ctx") * row_count
    query_pos = first_row + jnp.arange(row_count, dtype=jnp.int32)
    own_docs = doc_ids.astype(jnp.float32)
    weight_full = lax.all_gather(out_weight, "ctx", axis=0, tiled=True)
    packed = jnp.concatenate(
        [keys, values, doc_ids.astype(jnp.bfloat16)[:, None]], axis=1
    )
    gathered, slab = ctx_ring(packed, ctx_count)
    piece_rows = gathered.size // packed.shape[1]
    gathered = gathered.reshape(piece_rows, packed.shape[1])
    key_piece = gathered[:, :head_width]
    value_piece = gathered[:, head_width : 2 * head_width]
    doc_piece = gathered[:, 2 * head_width].astype(jnp.float32)
    slab = slab.reshape(-1)
    slab = jnp.where(slab >= 0, slab, 1 << 20)
    key_pos = (slab[:, None] * row_count + jnp.arange(row_count, dtype=jnp.int32)[None, :]).reshape(-1)
    allowed = (key_pos[None, :] <= query_pos[:, None]) & (
        doc_piece[None, :] == own_docs[:, None]
    )
    score = (
        jnp.einsum("id,jd->ij", query, key_piece, preferred_element_type=jnp.float32)
        * score_scale
    )
    distance = (query_pos[:, None] - key_pos[None, :]).astype(jnp.float32)
    score = score - alibi_slopes[0] * distance
    score = jnp.where(allowed, score, NEG_LARGE)
    best = jnp.max(score, axis=1)
    prob = jnp.where(allowed, jnp.exp(score - best[:, None]), 0.0)
    total = jnp.sum(prob, axis=1)
    mixed = jnp.einsum(
        "ij,jd->id", prob.astype(jnp.bfloat16), value_piece, preferred_element_type=jnp.float32
    )
    context = (mixed / total[:, None]).astype(jnp.bfloat16)
    context_all = gather_a2a(context, "dp", dp_count)
    context_all = context_all.transpose(1, 0, 2).reshape(row_count, dp_count * head_width)
    result = jnp.dot(context_all, weight_full, preferred_element_type=jnp.float32)
    return result.astype(jnp.bfloat16)


def solution(mesh):
    return jax.shard_map(
        shards,
        mesh=mesh,
        in_specs=(
            P("ctx", "dp"),
            P("ctx", "dp"),
            P("ctx", "dp"),
            P("ctx"),
            P("dp"),
            P("ctx", "dp"),
        ),
        out_specs=P("ctx", "dp"),
        check_vma=False,
    )
```

```python
import math

import jax
import jax.numpy as jnp
from jax import lax
from jax.sharding import PartitionSpec as P

NEG_LARGE = -1e30


def gather_a2a(block, axis, count):
    spread = jnp.broadcast_to(block[None], (count,) + block.shape)
    return lax.all_to_all(spread, axis, 0, 0, tiled=False)


def ctx_ring(block, ctx_count):
    rows = ctx_count // 4
    plane_size = 2 * rows

    def shifted(step):
        pairs = []
        for c in range(ctx_count):
            plane, row, core = c // plane_size, (c // 2) % rows, c % 2
            pairs.append((c, plane * plane_size + ((row + step) % rows) * 2 + core))
        return pairs

    partner = lax.ppermute(block, "ctx", [(c, c + plane_size) for c in range(plane_size)])
    payload = jnp.stack([block, partner])
    pieces, offsets = [payload], [0]
    current = payload
    for step in range(1, rows // 2 + 1):
        current = lax.ppermute(current, "ctx", shifted(1))
        pieces.append(current)
        offsets.append(-step)
    current = payload
    for step in range(1, (rows - 1) // 2 + 1):
        current = lax.ppermute(current, "ctx", shifted(-1))
        pieces.append(current)
        offsets.append(step)
    mine = jnp.stack(pieces)
    other = lax.ppermute(mine, "ctx", [(c, c ^ 1) for c in range(ctx_count)])
    gathered = jnp.stack([mine, other])
    me = lax.axis_index("ctx")
    plane, row, core = me // plane_size, (me // 2) % rows, me % 2
    src_row = (row + jnp.array(offsets, jnp.int32)) % rows
    src_core = jnp.array([0, 1], jnp.int32) ^ core
    slab = plane * plane_size + src_row[None, :, None] * 2 + src_core[:, None, None]
    slab = slab - jnp.array([0, plane_size], jnp.int32)[None, None, :]
    return gathered, slab


def shards(query, keys, values, doc_ids, alibi_slopes, out_weight):
    ctx_count = lax.axis_size("ctx")
    dp_count = lax.axis_size("dp")
    row_count = query.shape[0]
    head_width = query.shape[1]
    score_scale = 1.0 / math.sqrt(head_width)
    first_row = lax.axis_index("ctx") * row_count
    query_pos = first_row + jnp.arange(row_count, dtype=jnp.int32)
    own_docs = doc_ids.astype(jnp.float32)
    weight_full = lax.all_gather(out_weight, "ctx", axis=0, tiled=True)
    doc_column = doc_ids.astype(jnp.bfloat16)[:, None]
    packed = jnp.stack(
        [
            jnp.concatenate([keys, doc_column], axis=1),
            jnp.concatenate([values, jnp.zeros_like(doc_column)], axis=1),
        ]
    )
    gathered, slab = ctx_ring(packed, ctx_count)
    gathered = gathered.reshape((-1,) + packed.shape)
    key_blocks = gathered[:, 0, :, :head_width]
    value_blocks = gathered[:, 1, :, :head_width]
    doc_blocks = gathered[:, 0, :, head_width].astype(jnp.float32)
    slab = slab.reshape(-1)
    slab = jnp.where(slab >= 0, slab, 1 << 20)
    key_pos = slab[:, None] * row_count + jnp.arange(row_count, dtype=jnp.int32)[None, :]
    allowed = (key_pos[:, None, :] <= query_pos[None, :, None]) & (
        doc_blocks[:, None, :] == own_docs[None, :, None]
    )
    score = (
        jnp.einsum("id,bjd->bij", query, key_blocks, preferred_element_type=jnp.float32)
        * score_scale
    )
    distance = (query_pos[None, :, None] - key_pos[:, None, :]).astype(jnp.float32)
    score = score - alibi_slopes[0] * distance
    score = jnp.where(allowed, score, NEG_LARGE)
    best = jnp.max(score, axis=(0, 2))
    prob = jnp.where(allowed, jnp.exp(score - best[None, :, None]), 0.0)
    total = jnp.sum(prob, axis=(0, 2))
    mixed = jnp.einsum(
        "bij,bjd->id", prob.astype(jnp.bfloat16), value_blocks, preferred_element_type=jnp.float32
    )
    context = (mixed / total[:, None]).astype(jnp.bfloat16)
    context_all = gather_a2a(context, "dp", dp_count)
    weight_blocks = weight_full.reshape(dp_count, head_width, weight_full.shape[1])
    result = jnp.einsum(
        "bid,bdo->io", context_all, weight_blocks, preferred_element_type=jnp.float32
    )
    return result.astype(jnp.bfloat16)


def solution(mesh):
    return jax.shard_map(
        shards,
        mesh=mesh,
        in_specs=(
            P("ctx", "dp"),
            P("ctx", "dp"),
            P("ctx", "dp"),
            P("ctx"),
            P("dp"),
            P("ctx", "dp"),
        ),
        out_specs=P("ctx", "dp"),
        check_vma=False,
    )
```

```python
import math

import jax
import jax.numpy as jnp
from jax import lax
from jax.sharding import PartitionSpec as P

NEG_LARGE = -1e30


def gather_a2a(block, axis, count):
    spread = jnp.broadcast_to(block[None], (count,) + block.shape)
    return lax.all_to_all(spread, axis, 0, 0, tiled=False)


def ctx_ring(block, ctx_count):
    rows = ctx_count // 4
    plane_size = 2 * rows

    def shifted(step):
        pairs = []
        for c in range(ctx_count):
            plane, row, core = c // plane_size, (c // 2) % rows, c % 2
            pairs.append((c, plane * plane_size + ((row + step) % rows) * 2 + core))
        return pairs

    partner = lax.ppermute(block, "ctx", [(c, c + plane_size) for c in range(plane_size)])
    payload = jnp.stack([block, partner])
    pieces, offsets = [payload], [0]
    current = payload
    for step in range(1, rows // 2 + 1):
        current = lax.ppermute(current, "ctx", shifted(1))
        pieces.append(current)
        offsets.append(-step)
    current = payload
    for step in range(1, (rows - 1) // 2 + 1):
        current = lax.ppermute(current, "ctx", shifted(-1))
        pieces.append(current)
        offsets.append(step)
    mine = jnp.stack(pieces)
    other = lax.ppermute(mine, "ctx", [(c, c ^ 1) for c in range(ctx_count)])
    gathered = jnp.stack([mine, other])
    me = lax.axis_index("ctx")
    plane, row, core = me // plane_size, (me // 2) % rows, me % 2
    src_row = (row + jnp.array(offsets, jnp.int32)) % rows
    src_core = jnp.array([0, 1], jnp.int32) ^ core
    slab = plane * plane_size + src_row[None, :, None] * 2 + src_core[:, None, None]
    slab = slab - jnp.array([0, plane_size], jnp.int32)[None, None, :]
    return gathered, slab


def shards(query, keys, values, doc_ids, alibi_slopes, out_weight):
    ctx_count = lax.axis_size("ctx")
    dp_count = lax.axis_size("dp")
    row_count = query.shape[0]
    head_width = query.shape[1]
    score_scale = 1.0 / math.sqrt(head_width)
    first_row = lax.axis_index("ctx") * row_count
    query_pos = first_row + jnp.arange(row_count, dtype=jnp.int32)
    own_docs = doc_ids.astype(jnp.float32)
    weight_full = lax.all_gather(out_weight, "ctx", axis=0, tiled=True)
    doc_column = doc_ids.astype(jnp.bfloat16)[:, None]
    packed = jnp.stack(
        [
            jnp.concatenate([keys, doc_column], axis=1),
            jnp.concatenate([values, jnp.zeros_like(doc_column)], axis=1),
        ]
    )
    gathered, slab = ctx_ring(packed, ctx_count)
    gathered = gathered.reshape((-1,) + packed.shape)
    key_blocks = gathered[:, 0, :, :head_width]
    value_blocks = gathered[:, 1, :, :head_width]
    doc_blocks = gathered[:, 0, :, head_width].astype(jnp.float32)
    slab = slab.reshape(-1)
    slab = jnp.where(slab >= 0, slab, 1 << 20)
    key_pos = slab[:, None] * row_count + jnp.arange(row_count, dtype=jnp.int32)[None, :]
    allowed = (key_pos[:, None, :] <= query_pos[None, :, None]) & (
        doc_blocks[:, None, :] == own_docs[None, :, None]
    )
    score = (
        jnp.einsum("id,bjd->bij", query, key_blocks, preferred_element_type=jnp.float32)
        * score_scale
    )
    distance = (query_pos[None, :, None] - key_pos[:, None, :]).astype(jnp.float32)
    score = score - alibi_slopes[0] * distance
    score = jnp.where(allowed, score, NEG_LARGE)
    best = jnp.max(score, axis=(0, 2))
    prob = jnp.where(allowed, jnp.exp(score - best[None, :, None]), 0.0)
    total = jnp.sum(prob, axis=(0, 2))
    mixed = jnp.einsum(
        "bij,bjd->id", prob.astype(jnp.bfloat16), value_blocks, preferred_element_type=jnp.float32
    )
    context = (mixed / total[:, None]).astype(jnp.bfloat16)
    lanes = 128
    dense = context.reshape(context.size // lanes, lanes)
    context_all = gather_a2a(dense, "dp", dp_count).reshape((dp_count,) + context.shape)
    weight_blocks = weight_full.reshape(dp_count, head_width, weight_full.shape[1])
    result = jnp.einsum(
        "bid,bdo->io", context_all, weight_blocks, preferred_element_type=jnp.float32
    )
    return result.astype(jnp.bfloat16)


def solution(mesh):
    return jax.shard_map(
        shards,
        mesh=mesh,
        in_specs=(
            P("ctx", "dp"),
            P("ctx", "dp"),
            P("ctx", "dp"),
            P("ctx"),
            P("dp"),
            P("ctx", "dp"),
        ),
        out_specs=P("ctx", "dp"),
        check_vma=False,
    )
```

```python
import math

import jax
import jax.numpy as jnp
from jax import lax
from jax.sharding import PartitionSpec as P

NEG_LARGE = -1e30


def gather_a2a(block, axis, count):
    spread = jnp.broadcast_to(block[None], (count,) + block.shape)
    return lax.all_to_all(spread, axis, 0, 0, tiled=False)


def ctx_ring(block, ctx_count):
    rows = ctx_count // 4
    plane_size = 2 * rows

    def shifted(step):
        pairs = []
        for c in range(ctx_count):
            plane, row, core = c // plane_size, (c // 2) % rows, c % 2
            pairs.append((c, plane * plane_size + ((row + step) % rows) * 2 + core))
        return pairs

    partner = lax.ppermute(
        block, "ctx", [(c, (c + plane_size) % ctx_count) for c in range(ctx_count)]
    )
    payload = jnp.stack([block, partner])
    pieces, offsets = [payload], [0]
    current = payload
    for step in range(1, rows // 2 + 1):
        current = lax.ppermute(current, "ctx", shifted(1))
        pieces.append(current)
        offsets.append(-step)
    current = payload
    for step in range(1, (rows - 1) // 2 + 1):
        current = lax.ppermute(current, "ctx", shifted(-1))
        pieces.append(current)
        offsets.append(step)
    mine = jnp.stack(pieces)
    other = lax.ppermute(mine, "ctx", [(c, c ^ 1) for c in range(ctx_count)])
    gathered = jnp.stack([mine, other])
    me = lax.axis_index("ctx")
    plane, row, core = me // plane_size, (me // 2) % rows, me % 2
    src_row = (row + jnp.array(offsets, jnp.int32)) % rows
    src_core = jnp.array([0, 1], jnp.int32) ^ core
    slab = plane * plane_size + src_row[None, :, None] * 2 + src_core[:, None, None]
    slab = slab + jnp.array([0, plane_size], jnp.int32)[None, None, :]
    slab = slab % ctx_count
    return gathered, slab


def shards(query, keys, values, doc_ids, alibi_slopes, out_weight):
    ctx_count = lax.axis_size("ctx")
    dp_count = lax.axis_size("dp")
    row_count = query.shape[0]
    head_width = query.shape[1]
    score_scale = 1.0 / math.sqrt(head_width)
    first_row = lax.axis_index("ctx") * row_count
    query_pos = first_row + jnp.arange(row_count, dtype=jnp.int32)
    own_docs = doc_ids.astype(jnp.float32)
    doc_column = doc_ids.astype(jnp.bfloat16)[:, None]
    packed = jnp.stack(
        [
            jnp.concatenate([keys, doc_column], axis=1),
            jnp.concatenate([values, jnp.zeros_like(doc_column)], axis=1),
        ]
    )
    slot = packed.shape[1] * packed.shape[2]
    weight_flat = jnp.pad(out_weight.reshape(-1), (0, slot - out_weight.size))
    packed = jnp.concatenate([packed, weight_flat.reshape((1,) + packed.shape[1:])])
    gathered, slab = ctx_ring(packed, ctx_count)
    gathered = gathered.reshape((-1,) + packed.shape)
    key_blocks = gathered[:, 0, :, :head_width]
    value_blocks = gathered[:, 1, :, :head_width]
    doc_blocks = gathered[:, 0, :, head_width].astype(jnp.float32)
    slab = slab.reshape(-1)
    weight_blocks = (
        gathered[:, 2].reshape(gathered.shape[0], slot)[:, : out_weight.size].reshape(
            (gathered.shape[0],) + out_weight.shape
        )
    )
    key_pos = slab[:, None] * row_count + jnp.arange(row_count, dtype=jnp.int32)[None, :]
    allowed = (key_pos[:, None, :] <= query_pos[None, :, None]) & (
        doc_blocks[:, None, :] == own_docs[None, :, None]
    )
    score = (
        jnp.einsum("id,bjd->bij", query, key_blocks, preferred_element_type=jnp.float32)
        * score_scale
    )
    distance = (query_pos[None, :, None] - key_pos[:, None, :]).astype(jnp.float32)
    score = score - alibi_slopes[0] * distance
    score = jnp.where(allowed, score, NEG_LARGE)
    best = jnp.max(score, axis=(0, 2))
    prob = jnp.where(allowed, jnp.exp(score - best[None, :, None]), 0.0)
    total = jnp.sum(prob, axis=(0, 2))
    mixed = jnp.einsum(
        "bij,bjd->id", prob.astype(jnp.bfloat16), value_blocks, preferred_element_type=jnp.float32
    )
    context = (mixed / total[:, None]).astype(jnp.bfloat16)
    context_all = gather_a2a(context, "dp", dp_count)
    result = jnp.einsum(
        "bid,bdo->io", context_all[slab], weight_blocks, preferred_element_type=jnp.float32
    )
    return result.astype(jnp.bfloat16)


def solution(mesh):
    return jax.shard_map(
        shards,
        mesh=mesh,
        in_specs=(
            P("ctx", "dp"),
            P("ctx", "dp"),
            P("ctx", "dp"),
            P("ctx"),
            P("dp"),
            P("ctx", "dp"),
        ),
        out_specs=P("ctx", "dp"),
        check_vma=False,
    )
```

```python
import math

import jax
import jax.numpy as jnp
from jax import lax
from jax.sharding import PartitionSpec as P

NEG_LARGE = -1e30


def gather_a2a(block, axis, count):
    spread = jnp.broadcast_to(block[None], (count,) + block.shape)
    return lax.all_to_all(spread, axis, 0, 0, tiled=False)


def ctx_ring(block, ctx_count):
    rows = ctx_count // 4
    plane_size = 2 * rows

    def shifted(step):
        pairs = []
        for c in range(ctx_count):
            plane, row, core = c // plane_size, (c // 2) % rows, c % 2
            pairs.append((c, plane * plane_size + ((row + step) % rows) * 2 + core))
        return pairs

    partner = lax.ppermute(block, "ctx", [(c, c + plane_size) for c in range(plane_size)])
    payload = jnp.stack([block, partner])
    swap = [(c, c ^ 1) for c in range(ctx_count)]
    early, early_offsets = [payload], [0]
    current = payload
    for step in range(1, (rows - 1) // 2 + 1):
        current = lax.ppermute(current, "ctx", shifted(-1))
        early.append(current)
        early_offsets.append(step)
    late, late_offsets = [], []
    current = payload
    for step in range(1, rows // 2 + 1):
        current = lax.ppermute(current, "ctx", shifted(1))
        late.append(current)
        late_offsets.append(-step)
    early, late = jnp.stack(early), jnp.stack(late)
    other_early = lax.ppermute(early, "ctx", swap)
    other_late = lax.ppermute(late, "ctx", swap)
    mine = jnp.concatenate([early, late])
    other = jnp.concatenate([other_early, other_late])
    offsets = early_offsets + late_offsets
    gathered = jnp.stack([mine, other])
    me = lax.axis_index("ctx")
    plane, row, core = me // plane_size, (me // 2) % rows, me % 2
    src_row = (row + jnp.array(offsets, jnp.int32)) % rows
    src_core = jnp.array([0, 1], jnp.int32) ^ core
    slab = plane * plane_size + src_row[None, :, None] * 2 + src_core[:, None, None]
    slab = slab - jnp.array([0, plane_size], jnp.int32)[None, None, :]
    return gathered, slab


def shards(query, keys, values, doc_ids, alibi_slopes, out_weight):
    ctx_count = lax.axis_size("ctx")
    dp_count = lax.axis_size("dp")
    row_count = query.shape[0]
    head_width = query.shape[1]
    score_scale = 1.0 / math.sqrt(head_width)
    first_row = lax.axis_index("ctx") * row_count
    query_pos = first_row + jnp.arange(row_count, dtype=jnp.int32)
    own_docs = doc_ids.astype(jnp.float32)
    weight_full = lax.all_gather(out_weight, "ctx", axis=0, tiled=True)
    doc_column = doc_ids.astype(jnp.bfloat16)[:, None]
    packed = jnp.stack(
        [
            jnp.concatenate([keys, doc_column], axis=1),
            jnp.concatenate([values, jnp.zeros_like(doc_column)], axis=1),
        ]
    )
    gathered, slab = ctx_ring(packed, ctx_count)
    gathered = gathered.reshape((-1,) + packed.shape)
    key_blocks = gathered[:, 0, :, :head_width]
    value_blocks = gathered[:, 1, :, :head_width]
    doc_blocks = gathered[:, 0, :, head_width].astype(jnp.float32)
    slab = slab.reshape(-1)
    slab = jnp.where(slab >= 0, slab, 1 << 20)
    key_pos = slab[:, None] * row_count + jnp.arange(row_count, dtype=jnp.int32)[None, :]
    allowed = (key_pos[:, None, :] <= query_pos[None, :, None]) & (
        doc_blocks[:, None, :] == own_docs[None, :, None]
    )
    score = (
        jnp.einsum("id,bjd->bij", query, key_blocks, preferred_element_type=jnp.float32)
        * score_scale
    )
    distance = (query_pos[None, :, None] - key_pos[:, None, :]).astype(jnp.float32)
    score = score - alibi_slopes[0] * distance
    score = jnp.where(allowed, score, NEG_LARGE)
    best = jnp.max(score, axis=(0, 2))
    prob = jnp.where(allowed, jnp.exp(score - best[None, :, None]), 0.0)
    total = jnp.sum(prob, axis=(0, 2))
    mixed = jnp.einsum(
        "bij,bjd->id", prob.astype(jnp.bfloat16), value_blocks, preferred_element_type=jnp.float32
    )
    context = (mixed / total[:, None]).astype(jnp.bfloat16)
    context_all = gather_a2a(context, "dp", dp_count)
    weight_blocks = weight_full.reshape(dp_count, head_width, weight_full.shape[1])
    result = jnp.einsum(
        "bid,bdo->io", context_all, weight_blocks, preferred_element_type=jnp.float32
    )
    return result.astype(jnp.bfloat16)


def solution(mesh):
    return jax.shard_map(
        shards,
        mesh=mesh,
        in_specs=(
            P("ctx", "dp"),
            P("ctx", "dp"),
            P("ctx", "dp"),
            P("ctx"),
            P("dp"),
            P("ctx", "dp"),
        ),
        out_specs=P("ctx", "dp"),
        check_vma=False,
    )
```
